256 devices in a mesh: band: 16 (over y, x), slab: 16 (over z, core).
Axes of the slice: x: 4, y: 4, z: 8, core: 2. Of those that a mesh axis runs over, the one named last changes fastest.
Arguments:
- orbitals: bfloat16 [32, 16777216], P('band', 'slab'), may hold values from -6 to 6
- projectors: bfloat16 [16, 16, 512, 18, 128], P('slab', 'band'), may hold values from -0.5 to 0.5
- piece_block: int32 [16, 16, 512], P('slab', 'band'), may hold values from 0 to 511
- piece_atom: int32 [16, 16, 512], P('slab', 'band'), may hold values from -1 to 1151, as said below
- coupling: float32 [6144, 324], P('slab'), may hold values from -0.6 to 0.6
Outputs:
- applied: bfloat16 [32, 16777216], P('band', 'slab')
The draws below stay inside these ranges and needn't reach their ends.
Inputs may be any that keep to these rules, and one draw needn't show every extreme that they name: `piece_atom`: each entry is -1 (no atom) or side * 384 + slot with side in 0, 1, 2 and slot < 384: the atom in that slot of the slab side - 1 places away along the slab axis, cyclically. Slabs hold different numbers of atoms and of pieces with an atom.
All inputs are finite; a program needn't handle non-finite values.
Results may differ from the reference program's by a relative error of at most 0.0049.
Values may be sent and summed in bfloat16 or wider, within the bound.
No kernel may reach another device: no remote copies, remote signals or barrier semaphores. Data moves between devices by JAX's collectives and lax.ppermute only.
A program may use at most 128 MiB of HBM per device.

```python
import jax
import jax.numpy as jnp
from jax import lax

BANDS = 32
PROJ = 18
BLOCK = 128
PTS_DEV = 65536
PIECES = 512
ATOM_SLOTS = 384
NBLK = 512
GRID = 16777216
ATOMS = 6144
N_BAND = 16
N_SLAB = 16


def draw_piece_atom(key, part):
    key_count, key_side, key_slot, key_live = jax.random.split(jax.random.fold_in(key, 7), 4)
    counts = jax.random.randint(key_count, (N_SLAB,), ATOM_SLOTS // 4, ATOM_SLOTS + 1)
    counts = counts.at[0].set(ATOM_SLOTS)
    raw_side = jax.random.randint(key_side, (N_SLAB, N_BAND, PIECES), 0, 5)
    sides = jnp.where(raw_side == 0, 0, jnp.where(raw_side == 4, 2, 1))
    slab_ids = jnp.arange(N_SLAB, dtype=jnp.int32)[:, None, None]
    target = (slab_ids + sides - 1) % N_SLAB
    raw_slot = jax.random.randint(key_slot, (N_SLAB, N_BAND, PIECES), 0, ATOM_SLOTS)
    slot_ids = raw_slot % counts[target]
    live_draw = jax.random.randint(key_live, (N_SLAB, N_BAND, PIECES), 0, ATOM_SLOTS)
    is_live = live_draw < counts[slab_ids]
    values = jnp.where(is_live, sides * ATOM_SLOTS + slot_ids, -1)
    values = values.at[N_SLAB - 1, 0, 0].set(3 * ATOM_SLOTS - 1)
    values = values.at[0, 0, 1].set(-1)
    return values.astype(jnp.int32)


def set_ends(array, own_key, least, top_value):
    shape = array.shape
    index_at = [jax.random.randint(jax.random.fold_in(own_key, axis), (), 0, shape[axis]) for axis in range(len(shape))]
    array = array.at[tuple(index_at)].set(least)
    longest = shape.index(max(shape))
    index_at[longest] = (index_at[longest] + 1) % shape[longest]
    return array.at[tuple(index_at)].set(top_value)


def block_scale(rng, extent, shards, least, high):
    loudness, own = 1.0, jax.random.fold_in(rng, 6)
    for position, shards_of in shards:
        steps = jnp.exp(jax.random.uniform(jax.random.fold_in(own, position), (shards_of,), jnp.float32, least / len(shards), high / len(shards)))
        loudness = loudness * jnp.repeat(steps, extent[position] // shards_of).reshape([-1 if axis == position else 1 for axis in range(len(extent))])
    return loudness


def normal_values(key, shape, scale, most, pieces=(), kind=jnp.bfloat16):
    factor_of = block_scale(key, shape, pieces, -0.22, 0.18) if pieces else 1.0
    array = jax.random.normal(key, shape, jnp.float32) * scale * factor_of
    return jnp.minimum(jnp.maximum(array, -most), most).astype(kind)


def setup_inputs(seed: int = 0) -> dict:
    key_list = jax.random.split(jax.random.key(seed), 6)
    orbitals = normal_values(key_list[0], (BANDS, GRID), 1.0, 6.0, ((0, 16), (1, 16)))
    projectors = normal_values(key_list[1], (N_SLAB, N_BAND, PIECES, PROJ, BLOCK), BLOCK ** -0.5, 0.5, ((0, 16), (1, 16)))
    piece_block = set_ends(jax.random.randint(key_list[2], (N_SLAB, N_BAND, PIECES), 0, NBLK), jax.random.fold_in(key_list[2], 1), 0, NBLK - 1).astype(jnp.int32)
    piece_atom = draw_piece_atom(jax.random.fold_in(key_list[5], 71), 0)
    coupling = normal_values(key_list[4], (ATOMS, PROJ * PROJ), 0.1, 0.6, ((0, 16),), jnp.float32)
    return dict(orbitals=orbitals, projectors=projectors, piece_block=piece_block, piece_atom=piece_atom, coupling=coupling)


def reference(orbitals, projectors, piece_block, piece_atom, coupling):
    band_count = orbitals.shape[0]
    block_count = PTS_DEV // BLOCK
    device_count = N_SLAB * N_BAND
    grid_blocks = orbitals.reshape(band_count, device_count, block_count, BLOCK)
    device_blocks = jnp.moveaxis(grid_blocks, 1, 0)
    slab_ids = jnp.arange(N_SLAB, dtype=jnp.int32)[:, None, None]
    is_live = piece_atom >= 0
    sides = jnp.where(is_live, piece_atom // ATOM_SLOTS, 1).astype(jnp.int32)
    slot_ids = jnp.where(is_live, piece_atom % ATOM_SLOTS, 0).astype(jnp.int32)
    owner_slab = (slab_ids + sides - 1) % N_SLAB
    global_atom = jnp.where(is_live, owner_slab * ATOM_SLOTS + slot_ids, ATOMS).astype(jnp.int32)
    global_atom = global_atom.reshape(device_count, PIECES)
    proj_all = projectors.reshape(device_count, PIECES, PROJ, BLOCK)
    index_all = piece_block.reshape(device_count, PIECES).astype(jnp.int32)

    def project_one(items):
        blocks, proj_local, index_block = items
        picked = jnp.take(blocks, index_block, axis=1)
        return jnp.einsum("pjk,npk->pjn", proj_local.astype(jnp.float32), picked.astype(jnp.float32))

    terms = lax.map(project_one, (device_blocks, proj_all, index_all))
    coefs = jax.ops.segment_sum(terms.reshape(device_count * PIECES, PROJ * band_count),
                                global_atom.reshape(-1), num_segments=ATOMS + 1)[:ATOMS]
    coefs = coefs.reshape(ATOMS, PROJ, band_count)
    matrices = coupling.reshape(ATOMS, PROJ, PROJ)
    dressed = jnp.einsum("aij,ajn->ain", matrices, coefs, precision=lax.Precision.HIGHEST).astype(jnp.bfloat16)
    dressed_pad = jnp.concatenate([dressed, jnp.zeros((1, PROJ, band_count), jnp.bfloat16)], axis=0)

    def back_one(items):
        proj_local, index_block, atoms_local = items
        chosen = jnp.take(dressed_pad, atoms_local, axis=0)
        spread = jnp.einsum("pjk,pjn->npk", proj_local.astype(jnp.float32), chosen.astype(jnp.float32))
        result = jnp.zeros((band_count, block_count, BLOCK), jnp.float32).at[:, index_block].add(spread)
        return result.astype(jnp.bfloat16)

    pieces_out = lax.map(back_one, (proj_all, index_all, global_atom))
    return jnp.moveaxis(pieces_out, 0, 1).reshape(band_count, device_count * PTS_DEV)
```

```python
import jax
import jax.numpy as jnp
from jax import lax
from jax.experimental import pallas as pl
from jax.experimental.pallas import tpu as pltpu
from jax.sharding import PartitionSpec as P

PROJ = 18
BLOCK = 128


def shift(cells, axis, step):
    count = lax.axis_size(axis)
    return lax.ppermute(cells, axis, [(i, (i + step) % count) for i in range(count)])


def _scatter_body(blk_ref, spread_ref, out_ref, acc_ref):
    bands = out_ref.shape[0]
    blocks = out_ref.shape[1]
    acc_ref[...] = jnp.zeros(acc_ref.shape, jnp.float32)

    def step(p, carry):
        row = pl.multiple_of(blk_ref[p] * bands, bands)
        acc_ref[pl.ds(row, bands), :] += spread_ref[p]
        return carry

    lax.fori_loop(0, spread_ref.shape[0], step, 0, unroll=2)
    def emit(n, carry):
        out_ref[n] = acc_ref[pl.ds(n, blocks, stride=bands), :].astype(out_ref.dtype)
        return carry

    lax.fori_loop(0, bands, emit, 0)


def scatter_blocks(index_block, spread, block_count):
    pieces, bands, width = spread.shape
    return pl.pallas_call(
        _scatter_body,
        out_shape=jax.ShapeDtypeStruct((bands, block_count, width), jnp.bfloat16),
        in_specs=[
            pl.BlockSpec(memory_space=pltpu.SMEM),
            pl.BlockSpec(memory_space=pltpu.VMEM),
        ],
        out_specs=pl.BlockSpec(memory_space=pltpu.VMEM),
        scratch_shapes=[pltpu.VMEM((block_count * bands, width), jnp.float32)],
        compiler_params=pltpu.CompilerParams(vmem_limit_bytes=48 * 1024 * 1024),
    )(index_block, spread)


def body(orbitals, projectors, piece_block, piece_atom, coupling):
    slab_waves = lax.all_to_all(orbitals, "band", split_axis=1, concat_axis=0, tiled=True)
    band_count = slab_waves.shape[0]
    blocks = slab_waves.reshape(band_count, -1, BLOCK)
    block_count = blocks.shape[1]
    proj_local = projectors[0, 0]
    index_block = piece_block[0, 0]
    index_atom = piece_atom[0, 0]
    pieces = index_block.shape[0]
    slot_count = coupling.shape[0]
    is_live = index_atom >= 0
    picked = jnp.take(blocks, index_block, axis=1)
    projected = jnp.einsum("pjk,npk->pjn", proj_local, picked, preferred_element_type=jnp.float32)
    target = jnp.where(is_live, index_atom, 3 * slot_count)
    partial_value = jax.ops.segment_sum(
        projected.reshape(pieces, -1), target, num_segments=3 * slot_count + 1
    )
    partial_value = partial_value[: 3 * slot_count].reshape(3, slot_count, -1)
    own_total = (
        partial_value[1]
        + shift(partial_value[0], "slab", -1)
        + shift(partial_value[2], "slab", 1)
    )
    own_total = lax.psum(own_total, "band")
    matrices = coupling.reshape(slot_count, PROJ, PROJ)
    dressed = jnp.einsum(
        "aij,ajn->ain",
        matrices,
        own_total.reshape(slot_count, PROJ, band_count),
        precision=lax.Precision.HIGHEST,
    ).astype(jnp.bfloat16)
    flat_rows = jnp.concatenate(
        [shift(dressed, "slab", 1), dressed, shift(dressed, "slab", -1)], axis=0
    )
    chosen = jnp.take(flat_rows, jnp.where(is_live, index_atom, 0), axis=0)
    chosen = jnp.where(is_live[:, None, None], chosen, jnp.zeros((), jnp.bfloat16))
    spread = jnp.einsum("pjk,pjn->pnk", proj_local, chosen, preferred_element_type=jnp.float32)
    result = scatter_blocks(index_block, spread, block_count)
    result = result.reshape(band_count, -1)
    return lax.all_to_all(result, "band", split_axis=0, concat_axis=1, tiled=True)


def solution(mesh):
    placed = (
        P("band", "slab"),
        P("slab", "band", None, None, None),
        P("slab", "band", None),
        P("slab", "band", None),
        P("slab", None),
    )
    return jax.shard_map(
        body, mesh=mesh, in_specs=placed, out_specs=P("band", "slab"), check_vma=False
    )
```

```python
import jax
import jax.numpy as jnp
from jax import lax
from jax.experimental import pallas as pl
from jax.experimental.pallas import tpu as pltpu
from jax.sharding import PartitionSpec as P

PROJ = 18
BLOCK = 128


def shift(cells, axis, step):
    count = lax.axis_size(axis)
    return lax.ppermute(cells, axis, [(i, (i + step) % count) for i in range(count)])


def _scatter_body(blk_ref, spread_ref, out_ref, acc_ref):
    bands = out_ref.shape[0]
    blocks = out_ref.shape[1]
    acc_ref[...] = jnp.zeros(acc_ref.shape, jnp.float32)

    def step(p, carry):
        row = pl.multiple_of(blk_ref[p] * bands, bands)
        acc_ref[pl.ds(row, bands), :] += spread_ref[p]
        return carry

    lax.fori_loop(0, spread_ref.shape[0], step, 0, unroll=2)
    def emit(n, carry):
        out_ref[n] = acc_ref[pl.ds(n, blocks, stride=bands), :].astype(out_ref.dtype)
        return carry

    lax.fori_loop(0, bands, emit, 0)


def scatter_blocks(index_block, spread, block_count):
    pieces, bands, width = spread.shape
    return pl.pallas_call(
        _scatter_body,
        out_shape=jax.ShapeDtypeStruct((bands, block_count, width), jnp.bfloat16),
        in_specs=[
            pl.BlockSpec(memory_space=pltpu.SMEM),
            pl.BlockSpec(memory_space=pltpu.VMEM),
        ],
        out_specs=pl.BlockSpec(memory_space=pltpu.VMEM),
        scratch_shapes=[pltpu.VMEM((block_count * bands, width), jnp.float32)],
        compiler_params=pltpu.CompilerParams(vmem_limit_bytes=48 * 1024 * 1024),
    )(index_block, spread)


def body(orbitals, projectors, piece_block, piece_atom, coupling):
    slab_waves = lax.all_to_all(orbitals, "band", split_axis=1, concat_axis=0, tiled=True)
    band_count = slab_waves.shape[0]
    blocks = slab_waves.reshape(band_count, -1, BLOCK)
    block_count = blocks.shape[1]
    proj_local = projectors[0, 0]
    index_block = piece_block[0, 0]
    index_atom = piece_atom[0, 0]
    pieces = index_block.shape[0]
    slot_count = coupling.shape[0]
    is_live = index_atom >= 0
    picked = jnp.take(blocks, index_block, axis=1)
    projected = jnp.einsum("pjk,npk->pjn", proj_local, picked, preferred_element_type=jnp.float32)
    target = jnp.where(is_live, index_atom, 3 * slot_count)
    partial_value = jax.ops.segment_sum(
        projected.reshape(pieces, -1), target, num_segments=3 * slot_count + 1
    )
    partial_value = partial_value[: 3 * slot_count].reshape(3, slot_count, -1)
    own_total = (
        partial_value[1]
        + shift(partial_value[0], "slab", -1)
        + shift(partial_value[2], "slab", 1)
    )
    band_size = lax.axis_size("band")
    share = slot_count // band_size
    arrived = lax.all_to_all(
        own_total.reshape(band_size, share, -1), "band", split_axis=0, concat_axis=0, tiled=True
    )
    mine = arrived.sum(axis=0)
    first = lax.axis_index("band") * share
    matrices = lax.dynamic_slice_in_dim(coupling, first, share, axis=0).reshape(share, PROJ, PROJ)
    dressed = jnp.einsum(
        "aij,ajn->ain",
        matrices,
        mine.reshape(share, PROJ, band_count),
        precision=lax.Precision.HIGHEST,
    ).astype(jnp.bfloat16)
    sides = jnp.stack([shift(dressed, "slab", 1), dressed, shift(dressed, "slab", -1)])
    spread_out = jnp.broadcast_to(sides[None], (band_size,) + sides.shape)
    every = lax.all_to_all(spread_out, "band", split_axis=0, concat_axis=0, tiled=True)
    flat_rows = jnp.swapaxes(every, 0, 1).reshape(3 * slot_count, PROJ, band_count)
    chosen = jnp.take(flat_rows, jnp.where(is_live, index_atom, 0), axis=0)
    chosen = jnp.where(is_live[:, None, None], chosen, jnp.zeros((), jnp.bfloat16))
    spread = jnp.einsum("pjk,pjn->pnk", proj_local, chosen, preferred_element_type=jnp.float32)
    result = scatter_blocks(index_block, spread, block_count)
    result = result.reshape(band_count, -1)
    return lax.all_to_all(result, "band", split_axis=0, concat_axis=1, tiled=True)


def solution(mesh):
    placed = (
        P("band", "slab"),
        P("slab", "band", None, None, None),
        P("slab", "band", None),
        P("slab", "band", None),
        P("slab", None),
    )
    return jax.shard_map(
        body, mesh=mesh, in_specs=placed, out_specs=P("band", "slab"), check_vma=False
    )
```

```python
import jax
import jax.numpy as jnp
from jax import lax
from jax.experimental import pallas as pl
from jax.experimental.pallas import tpu as pltpu
from jax.sharding import PartitionSpec as P

PROJ = 18
BLOCK = 128


def shift(cells, axis, step):
    count = lax.axis_size(axis)
    return lax.ppermute(cells, axis, [(i, (i + step) % count) for i in range(count)])


def _scatter_body(blk_ref, spread_ref, out_ref, acc_ref):
    bands = out_ref.shape[0]
    blocks = out_ref.shape[1]
    acc_ref[...] = jnp.zeros(acc_ref.shape, jnp.float32)

    def step(p, carry):
        row = pl.multiple_of(blk_ref[p] * bands, bands)
        acc_ref[pl.ds(row, bands), :] += spread_ref[p]
        return carry

    lax.fori_loop(0, spread_ref.shape[0], step, 0, unroll=2)
    def emit(n, carry):
        out_ref[n] = acc_ref[pl.ds(n, blocks, stride=bands), :].astype(out_ref.dtype)
        return carry

    lax.fori_loop(0, bands, emit, 0)


def scatter_blocks(index_block, spread, block_count):
    pieces, bands, width = spread.shape
    return pl.pallas_call(
        _scatter_body,
        out_shape=jax.ShapeDtypeStruct((bands, block_count, width), jnp.bfloat16),
        in_specs=[
            pl.BlockSpec(memory_space=pltpu.SMEM),
            pl.BlockSpec(memory_space=pltpu.VMEM),
        ],
        out_specs=pl.BlockSpec(memory_space=pltpu.VMEM),
        scratch_shapes=[pltpu.VMEM((block_count * bands, width), jnp.float32)],
        compiler_params=pltpu.CompilerParams(vmem_limit_bytes=48 * 1024 * 1024),
    )(index_block, spread)


def body(orbitals, projectors, piece_block, piece_atom, coupling):
    band_size = lax.axis_size("band")
    local_bands = orbitals.shape[0]
    band_count = band_size * local_bands
    proj_local = projectors[0, 0]
    index_block = piece_block[0, 0]
    index_atom = piece_atom[0, 0]
    pieces = index_block.shape[0]
    slot_count = coupling.shape[0]
    is_live = index_atom >= 0
    target = jnp.where(is_live, index_atom, 3 * slot_count)
    halves = []
    for c in range(local_bands):
        got = lax.all_to_all(
            orbitals[c].reshape(band_size, -1), "band", split_axis=0, concat_axis=0, tiled=True
        )
        blocks = got.reshape(band_size, -1, BLOCK)
        block_count = blocks.shape[1]
        picked = jnp.take(blocks, index_block, axis=1)
        projected = jnp.einsum(
            "pjk,npk->pjn", proj_local, picked, preferred_element_type=jnp.float32
        )
        summed = jax.ops.segment_sum(
            projected.reshape(pieces, -1), target, num_segments=3 * slot_count + 1
        )
        halves.append(summed[: 3 * slot_count].reshape(3 * slot_count, PROJ, band_size))
    partial_value = jnp.concatenate(halves, axis=-1).reshape(3, slot_count, -1)
    own_total = (
        partial_value[1]
        + shift(partial_value[0], "slab", -1)
        + shift(partial_value[2], "slab", 1)
    )
    share = slot_count // band_size
    arrived = lax.all_to_all(
        own_total.reshape(band_size, share, -1), "band", split_axis=0, concat_axis=0, tiled=True
    )
    mine = arrived.sum(axis=0)
    first = lax.axis_index("band") * share
    matrices = lax.dynamic_slice_in_dim(coupling, first, share, axis=0).reshape(share, PROJ, PROJ)
    dressed = jnp.einsum(
        "aij,ajn->ain",
        matrices,
        mine.reshape(share, PROJ, band_count),
        precision=lax.Precision.HIGHEST,
    ).astype(jnp.bfloat16)
    sides = jnp.stack([shift(dressed, "slab", 1), dressed, shift(dressed, "slab", -1)])
    spread_out = jnp.broadcast_to(sides[None], (band_size,) + sides.shape)
    every = lax.all_to_all(spread_out, "band", split_axis=0, concat_axis=0, tiled=True)
    flat_rows = jnp.swapaxes(every, 0, 1).reshape(3 * slot_count, PROJ, band_count)
    chosen = jnp.take(flat_rows, jnp.where(is_live, index_atom, 0), axis=0)
    chosen = jnp.where(is_live[:, None, None], chosen, jnp.zeros((), jnp.bfloat16))
    outs = []
    for c in range(local_bands):
        spread = jnp.einsum(
            "pjk,pjn->pnk",
            proj_local,
            chosen[:, :, c * band_size : (c + 1) * band_size],
            preferred_element_type=jnp.float32,
        )
        result = scatter_blocks(index_block, spread, block_count)
        sent = lax.all_to_all(
            result.reshape(band_size, -1), "band", split_axis=0, concat_axis=0, tiled=True
        )
        outs.append(sent.reshape(-1))
    return jnp.stack(outs)


def solution(mesh):
    placed = (
        P("band", "slab"),
        P("slab", "band", None, None, None),
        P("slab", "band", None),
        P("slab", "band", None),
        P("slab", None),
    )
    return jax.shard_map(
        body, mesh=mesh, in_specs=placed, out_specs=P("band", "slab"), check_vma=False
    )
```

```python
import jax
import jax.numpy as jnp
from jax import lax
from jax.experimental import pallas as pl
from jax.experimental.pallas import tpu as pltpu
from jax.sharding import PartitionSpec as P

PROJ = 18
BLOCK = 128


def shift(cells, axis, step):
    count = lax.axis_size(axis)
    return lax.ppermute(cells, axis, [(i, (i + step) % count) for i in range(count)])


def _scatter_body(blk_ref, spread_ref, out_ref, acc_ref):
    bands = out_ref.shape[0]
    blocks = out_ref.shape[1]
    acc_ref[...] = jnp.zeros(acc_ref.shape, jnp.float32)

    def step(p, carry):
        row = pl.multiple_of(blk_ref[p] * bands, bands)
        acc_ref[pl.ds(row, bands), :] += spread_ref[p]
        return carry

    lax.fori_loop(0, spread_ref.shape[0], step, 0, unroll=2)
    def emit(n, carry):
        out_ref[n] = acc_ref[pl.ds(n, blocks, stride=bands), :].astype(out_ref.dtype)
        return carry

    lax.fori_loop(0, bands, emit, 0)


def scatter_blocks(index_block, spread, block_count):
    pieces, bands, width = spread.shape
    return pl.pallas_call(
        _scatter_body,
        out_shape=jax.ShapeDtypeStruct((bands, block_count, width), jnp.bfloat16),
        in_specs=[
            pl.BlockSpec(memory_space=pltpu.SMEM),
            pl.BlockSpec(memory_space=pltpu.VMEM),
        ],
        out_specs=pl.BlockSpec(memory_space=pltpu.VMEM),
        scratch_shapes=[pltpu.VMEM((block_count * bands, width), jnp.float32)],
        compiler_params=pltpu.CompilerParams(vmem_limit_bytes=48 * 1024 * 1024),
    )(index_block, spread)


def body(orbitals, projectors, piece_block, piece_atom, coupling):
    slab_waves = lax.all_to_all(orbitals, "band", split_axis=1, concat_axis=0, tiled=True)
    band_count = slab_waves.shape[0]
    blocks = slab_waves.reshape(band_count, -1, BLOCK)
    block_count = blocks.shape[1]
    proj_local = projectors[0, 0]
    index_block = piece_block[0, 0]
    index_atom = piece_atom[0, 0]
    pieces = index_block.shape[0]
    slot_count = coupling.shape[0]
    is_live = index_atom >= 0
    picked = jnp.take(blocks, index_block, axis=1)
    projected = jnp.einsum("pjk,npk->pjn", proj_local, picked, preferred_element_type=jnp.float32)
    target = jnp.where(is_live, index_atom, 3 * slot_count)
    partial_value = jax.ops.segment_sum(
        projected.reshape(pieces, -1), target, num_segments=3 * slot_count + 1
    )
    partial_value = partial_value[: 3 * slot_count].reshape(3, slot_count, -1)
    own_total = (
        partial_value[1]
        + shift(partial_value[0], "slab", -1)
        + shift(partial_value[2], "slab", 1)
    )
    band_size = lax.axis_size("band")
    share = slot_count // band_size
    arrived = lax.all_to_all(
        own_total.reshape(band_size, share, -1), "band", split_axis=0, concat_axis=0, tiled=True
    )
    mine = arrived.sum(axis=0)
    first = lax.axis_index("band") * share
    matrices = lax.dynamic_slice_in_dim(coupling, first, share, axis=0).reshape(share, PROJ, PROJ)
    dressed = jnp.einsum(
        "aij,ajn->ain",
        matrices,
        mine.reshape(share, PROJ, band_count),
        precision=lax.Precision.HIGHEST,
    ).astype(jnp.bfloat16).reshape(share, PROJ * band_count)
    sides = jnp.stack([shift(dressed, "slab", 1), dressed, shift(dressed, "slab", -1)])
    spread_out = jnp.broadcast_to(sides.reshape(1, -1), (band_size, sides.size))
    every = lax.all_to_all(spread_out, "band", split_axis=0, concat_axis=0, tiled=True)
    rows = every.reshape(band_size * 3 * share, PROJ * band_count)
    side_of = index_atom // slot_count
    slot_of = index_atom % slot_count
    row_of = (slot_of // share) * (3 * share) + side_of * share + slot_of % share
    chosen = jnp.take(rows, jnp.where(is_live, row_of, 0), axis=0)
    chosen = jnp.where(is_live[:, None], chosen, jnp.zeros((), jnp.bfloat16))
    chosen = chosen.reshape(pieces, PROJ, band_count)
    spread = jnp.einsum("pjk,pjn->pnk", proj_local, chosen, preferred_element_type=jnp.float32)
    result = scatter_blocks(index_block, spread, block_count)
    result = result.reshape(band_count, -1)
    return lax.all_to_all(result, "band", split_axis=0, concat_axis=1, tiled=True)


def solution(mesh):
    placed = (
        P("band", "slab"),
        P("slab", "band", None, None, None),
        P("slab", "band", None),
        P("slab", "band", None),
        P("slab", None),
    )
    return jax.shard_map(
        body, mesh=mesh, in_specs=placed, out_specs=P("band", "slab"), check_vma=False
    )
```

```python
import jax
import jax.numpy as jnp
from jax import lax
from jax.experimental import pallas as pl
from jax.experimental.pallas import tpu as pltpu
from jax.sharding import PartitionSpec as P

PROJ = 18
BLOCK = 128


def shift(cells, axis, step):
    count = lax.axis_size(axis)
    return lax.ppermute(cells, axis, [(i, (i + step) % count) for i in range(count)])


def _scatter_body(blk_ref, spread_ref, out_ref, acc_ref):
    bands = out_ref.shape[0]
    blocks = out_ref.shape[1]
    acc_ref[...] = jnp.zeros(acc_ref.shape, jnp.float32)

    def step(p, carry):
        row = pl.multiple_of(blk_ref[p] * bands, bands)
        acc_ref[pl.ds(row, bands), :] += spread_ref[p]
        return carry

    lax.fori_loop(0, spread_ref.shape[0], step, 0, unroll=2)
    def emit(n, carry):
        out_ref[n] = acc_ref[pl.ds(n, blocks, stride=bands), :].astype(out_ref.dtype)
        return carry

    lax.fori_loop(0, bands, emit, 0)


def scatter_blocks(index_block, spread, block_count):
    pieces, bands, width = spread.shape
    return pl.pallas_call(
        _scatter_body,
        out_shape=jax.ShapeDtypeStruct((bands, block_count, width), jnp.bfloat16),
        in_specs=[
            pl.BlockSpec(memory_space=pltpu.SMEM),
            pl.BlockSpec(memory_space=pltpu.VMEM),
        ],
        out_specs=pl.BlockSpec(memory_space=pltpu.VMEM),
        scratch_shapes=[pltpu.VMEM((block_count * bands, width), jnp.float32)],
        compiler_params=pltpu.CompilerParams(vmem_limit_bytes=48 * 1024 * 1024),
    )(index_block, spread)


def body(orbitals, projectors, piece_block, piece_atom, coupling):
    slab_waves = lax.all_to_all(orbitals, "band", split_axis=1, concat_axis=0, tiled=True)
    band_count = slab_waves.shape[0]
    blocks = slab_waves.reshape(band_count, -1, BLOCK)
    block_count = blocks.shape[1]
    proj_local = projectors[0, 0]
    index_block = piece_block[0, 0]
    index_atom = piece_atom[0, 0]
    pieces = index_block.shape[0]
    slot_count = coupling.shape[0]
    is_live = index_atom >= 0
    picked = jnp.take(blocks, index_block, axis=1)
    projected = jnp.einsum("pjk,npk->pjn", proj_local, picked, preferred_element_type=jnp.float32)
    target = jnp.where(is_live, index_atom, 3 * slot_count)
    partial_value = jax.ops.segment_sum(
        projected.reshape(pieces, -1), target, num_segments=3 * slot_count + 1
    )
    partial_value = partial_value[: 3 * slot_count].reshape(3, slot_count, -1)
    own_total = (
        partial_value[1]
        + shift(partial_value[0], "slab", -1)
        + shift(partial_value[2], "slab", 1)
    )
    band_size = lax.axis_size("band")
    share = slot_count // band_size
    arrived = lax.all_to_all(
        own_total.reshape(band_size, share, -1), "band", split_axis=0, concat_axis=0, tiled=True
    )
    mine = arrived.sum(axis=0)
    first = lax.axis_index("band") * share
    matrices = lax.dynamic_slice_in_dim(coupling, first, share, axis=0).reshape(share, PROJ, PROJ)
    dressed = jnp.einsum(
        "aij,ajn->ain",
        matrices,
        mine.reshape(share, PROJ, band_count),
        precision=lax.Precision.HIGHEST,
    ).astype(jnp.bfloat16).reshape(share, PROJ * band_count)
    every = jnp.concatenate([shift(dressed, "slab", 1), dressed, shift(dressed, "slab", -1)])
    mask = 1
    while mask < band_size:
        swap = [(i, i ^ mask) for i in range(band_size)]
        every = jnp.concatenate([every, lax.ppermute(every, "band", swap)])
        mask *= 2
    side_of = index_atom // slot_count
    slot_of = index_atom % slot_count
    place = lax.axis_index("band") ^ (slot_of // share)
    row_of = place * (3 * share) + side_of * share + slot_of % share
    chosen = jnp.take(every, jnp.where(is_live, row_of, 0), axis=0)
    chosen = jnp.where(is_live[:, None], chosen, jnp.zeros((), jnp.bfloat16))
    chosen = chosen.reshape(pieces, PROJ, band_count)
    spread = jnp.einsum("pjk,pjn->pnk", proj_local, chosen, preferred_element_type=jnp.float32)
    result = scatter_blocks(index_block, spread, block_count)
    result = result.reshape(band_count, -1)
    return lax.all_to_all(result, "band", split_axis=0, concat_axis=1, tiled=True)


def solution(mesh):
    placed = (
        P("band", "slab"),
        P("slab", "band", None, None, None),
        P("slab", "band", None),
        P("slab", "band", None),
        P("slab", None),
    )
    return jax.shard_map(
        body, mesh=mesh, in_specs=placed, out_specs=P("band", "slab"), check_vma=False
    )
```

```python
import jax
import jax.numpy as jnp
from jax import lax
from jax.experimental import pallas as pl
from jax.experimental.pallas import tpu as pltpu
from jax.sharding import PartitionSpec as P

PROJ = 18
BLOCK = 128


def shift(cells, axis, step):
    count = lax.axis_size(axis)
    return lax.ppermute(cells, axis, [(i, (i + step) % count) for i in range(count)])


def doubling_masks(count):
    masks = [1 << k for k in range(count.bit_length() - 1)]
    far = [m for k, m in enumerate(masks) if k % 2 == 1]
    near = [m for k, m in enumerate(masks) if k % 2 == 0]
    return far + near


def _scatter_body(blk_ref, spread_ref, out_ref, acc_ref):
    bands = out_ref.shape[0]
    blocks = out_ref.shape[1]
    acc_ref[...] = jnp.zeros(acc_ref.shape, jnp.float32)

    def step(p, carry):
        row = pl.multiple_of(blk_ref[p] * bands, bands)
        acc_ref[pl.ds(row, bands), :] += spread_ref[p]
        return carry

    lax.fori_loop(0, spread_ref.shape[0], step, 0, unroll=2)
    def emit(n, carry):
        out_ref[n] = acc_ref[pl.ds(n, blocks, stride=bands), :].astype(out_ref.dtype)
        return carry

    lax.fori_loop(0, bands, emit, 0)


def scatter_blocks(index_block, spread, block_count):
    pieces, bands, width = spread.shape
    return pl.pallas_call(
        _scatter_body,
        out_shape=jax.ShapeDtypeStruct((bands, block_count, width), jnp.bfloat16),
        in_specs=[
            pl.BlockSpec(memory_space=pltpu.SMEM),
            pl.BlockSpec(memory_space=pltpu.VMEM),
        ],
        out_specs=pl.BlockSpec(memory_space=pltpu.VMEM),
        scratch_shapes=[pltpu.VMEM((block_count * bands, width), jnp.float32)],
        compiler_params=pltpu.CompilerParams(vmem_limit_bytes=48 * 1024 * 1024),
    )(index_block, spread)


def body(orbitals, projectors, piece_block, piece_atom, coupling):
    slab_waves = lax.all_to_all(orbitals, "band", split_axis=1, concat_axis=0, tiled=True)
    band_count = slab_waves.shape[0]
    blocks = slab_waves.reshape(band_count, -1, BLOCK)
    block_count = blocks.shape[1]
    proj_local = projectors[0, 0]
    index_block = piece_block[0, 0]
    index_atom = piece_atom[0, 0]
    pieces = index_block.shape[0]
    slot_count = coupling.shape[0]
    is_live = index_atom >= 0
    picked = jnp.take(blocks, index_block, axis=1)
    projected = jnp.einsum("pjk,npk->pjn", proj_local, picked, preferred_element_type=jnp.float32)
    target = jnp.where(is_live, index_atom, 3 * slot_count)
    partial_value = jax.ops.segment_sum(
        projected.reshape(pieces, -1), target, num_segments=3 * slot_count + 1
    )
    partial_value = partial_value[: 3 * slot_count].reshape(3, slot_count, -1)
    own_total = (
        partial_value[1]
        + shift(partial_value[0], "slab", -1)
        + shift(partial_value[2], "slab", 1)
    )
    band_size = lax.axis_size("band")
    share = slot_count // band_size
    arrived = lax.all_to_all(
        own_total.reshape(band_size, share, -1), "band", split_axis=0, concat_axis=0, tiled=True
    )
    mine = arrived.sum(axis=0)
    first = lax.axis_index("band") * share
    matrices = lax.dynamic_slice_in_dim(coupling, first, share, axis=0).reshape(share, PROJ, PROJ)
    dressed = jnp.einsum(
        "aij,ajn->ain",
        matrices,
        mine.reshape(share, PROJ, band_count),
        precision=lax.Precision.HIGHEST,
    ).astype(jnp.bfloat16).reshape(share, PROJ * band_count)
    every = jnp.concatenate([shift(dressed, "slab", 1), dressed, shift(dressed, "slab", -1)])
    masks = doubling_masks(band_size)
    for mask in masks:
        swap = [(i, i ^ mask) for i in range(band_size)]
        every = jnp.concatenate([every, lax.ppermute(every, "band", swap)])
    side_of = index_atom // slot_count
    slot_of = index_atom % slot_count
    apart = lax.axis_index("band") ^ (slot_of // share)
    place = sum(((apart // mask) % 2) << step for step, mask in enumerate(masks))
    row_of = place * (3 * share) + side_of * share + slot_of % share
    chosen = jnp.take(every, jnp.where(is_live, row_of, 0), axis=0)
    chosen = jnp.where(is_live[:, None], chosen, jnp.zeros((), jnp.bfloat16))
    chosen = chosen.reshape(pieces, PROJ, band_count)
    spread = jnp.einsum("pjk,pjn->pnk", proj_local, chosen, preferred_element_type=jnp.float32)
    result = scatter_blocks(index_block, spread, block_count)
    result = result.reshape(band_count, -1)
    return lax.all_to_all(result, "band", split_axis=0, concat_axis=1, tiled=True)


def solution(mesh):
    placed = (
        P("band", "slab"),
        P("slab", "band", None, None, None),
        P("slab", "band", None),
        P("slab", "band", None),
        P("slab", None),
    )
    return jax.shard_map(
        body, mesh=mesh, in_specs=placed, out_specs=P("band", "slab"), check_vma=False
    )
```

```python
import jax
import jax.numpy as jnp
from jax import lax
from jax.experimental import pallas as pl
from jax.experimental.pallas import tpu as pltpu
from jax.sharding import PartitionSpec as P

PROJ = 18
BLOCK = 128


def shift(cells, axis, step):
    count = lax.axis_size(axis)
    return lax.ppermute(cells, axis, [(i, (i + step) % count) for i in range(count)])


RING = 4
TILE_ROWS = 16


def ring_gather(rows, stride, count, split):
    def step(cells, delta):
        pairs = []
        for i in range(count):
            coord = (i // stride) % RING
            pairs.append((i, i + (((coord + delta) % RING) - coord) * stride))
        return lax.ppermute(cells, "band", pairs)

    left = step(rows, 1)
    right = step(rows, -1)
    if split:
        half = rows.shape[0] // 2
        return jnp.concatenate([rows, left, right, step(left[:half], 1), step(right[half:], -1)])
    return jnp.concatenate([rows, left, right, step(left, 1)])


def _scatter_body(blk_ref, spread_ref, out_ref, acc_ref):
    bands = out_ref.shape[0]
    blocks = out_ref.shape[1]
    acc_ref[...] = jnp.zeros(acc_ref.shape, jnp.float32)

    def step(p, carry):
        row = pl.multiple_of(blk_ref[p] * bands, bands)
        acc_ref[pl.ds(row, bands), :] += spread_ref[p]
        return carry

    lax.fori_loop(0, spread_ref.shape[0], step, 0, unroll=2)
    def emit(n, carry):
        out_ref[n] = acc_ref[pl.ds(n, blocks, stride=bands), :].astype(out_ref.dtype)
        return carry

    lax.fori_loop(0, bands, emit, 0)


def scatter_blocks(index_block, spread, block_count):
    pieces, bands, width = spread.shape
    return pl.pallas_call(
        _scatter_body,
        out_shape=jax.ShapeDtypeStruct((bands, block_count, width), jnp.bfloat16),
        in_specs=[
            pl.BlockSpec(memory_space=pltpu.SMEM),
            pl.BlockSpec(memory_space=pltpu.VMEM),
        ],
        out_specs=pl.BlockSpec(memory_space=pltpu.VMEM),
        scratch_shapes=[pltpu.VMEM((block_count * bands, width), jnp.float32)],
        compiler_params=pltpu.CompilerParams(vmem_limit_bytes=48 * 1024 * 1024),
    )(index_block, spread)


def body(orbitals, projectors, piece_block, piece_atom, coupling):
    slab_waves = lax.all_to_all(orbitals, "band", split_axis=1, concat_axis=0, tiled=True)
    band_count = slab_waves.shape[0]
    blocks = slab_waves.reshape(band_count, -1, BLOCK)
    block_count = blocks.shape[1]
    proj_local = projectors[0, 0]
    index_block = piece_block[0, 0]
    index_atom = piece_atom[0, 0]
    pieces = index_block.shape[0]
    slot_count = coupling.shape[0]
    is_live = index_atom >= 0
    picked = jnp.take(blocks, index_block, axis=1)
    projected = jnp.einsum("pjk,npk->pjn", proj_local, picked, preferred_element_type=jnp.float32)
    target = jnp.where(is_live, index_atom, 3 * slot_count)
    partial_value = jax.ops.segment_sum(
        projected.reshape(pieces, -1), target, num_segments=3 * slot_count + 1
    )
    partial_value = partial_value[: 3 * slot_count].reshape(3, slot_count, -1)
    own_total = (
        partial_value[1]
        + shift(partial_value[0], "slab", -1)
        + shift(partial_value[2], "slab", 1)
    )
    band_size = lax.axis_size("band")
    share = slot_count // band_size
    arrived = lax.all_to_all(
        own_total.reshape(band_size, share, -1), "band", split_axis=0, concat_axis=0, tiled=True
    )
    mine = arrived.sum(axis=0)
    first = lax.axis_index("band") * share
    matrices = lax.dynamic_slice_in_dim(coupling, first, share, axis=0).reshape(share, PROJ, PROJ)
    dressed = jnp.einsum(
        "aij,ajn->ain",
        matrices,
        mine.reshape(share, PROJ, band_count),
        precision=lax.Precision.HIGHEST,
    ).astype(jnp.bfloat16).reshape(share, PROJ * band_count)
    every = jnp.concatenate([shift(dressed, "slab", 1), dressed, shift(dressed, "slab", -1)])
    block_rows = -(-every.shape[0] // TILE_ROWS) * TILE_ROWS
    every = jnp.pad(every, ((0, block_rows - every.shape[0]), (0, 0)))
    every = ring_gather(every, 1, band_size, False)
    every = ring_gather(every, RING, band_size, True)
    side_of = index_atom // slot_count
    slot_of = index_atom % slot_count
    source = slot_of // share
    me = lax.axis_index("band")
    order = jnp.array([0, 2, 3, 1], jnp.int32)
    place_x = order[(source % RING - me % RING) % RING]
    place_y = order[(source // RING - me // RING) % RING]
    place = place_y * RING + place_x
    row_of = place * block_rows + side_of * share + slot_of % share
    chosen = jnp.take(every, jnp.where(is_live, row_of, 0), axis=0)
    chosen = jnp.where(is_live[:, None], chosen, jnp.zeros((), jnp.bfloat16))
    chosen = chosen.reshape(pieces, PROJ, band_count)
    spread = jnp.einsum("pjk,pjn->pnk", proj_local, chosen, preferred_element_type=jnp.float32)
    result = scatter_blocks(index_block, spread, block_count)
    result = result.reshape(band_count, -1)
    return lax.all_to_all(result, "band", split_axis=0, concat_axis=1, tiled=True)


def solution(mesh):
    placed = (
        P("band", "slab"),
        P("slab", "band", None, None, None),
        P("slab", "band", None),
        P("slab", "band", None),
        P("slab", None),
    )
    return jax.shard_map(
        body, mesh=mesh, in_specs=placed, out_specs=P("band", "slab"), check_vma=False
    )
```

```python
import jax
import jax.numpy as jnp
from jax import lax
from jax.experimental import pallas as pl
from jax.experimental.pallas import tpu as pltpu
from jax.sharding import PartitionSpec as P

PROJ = 18
BLOCK = 128


def shift(cells, axis, step):
    count = lax.axis_size(axis)
    return lax.ppermute(cells, axis, [(i, (i + step) % count) for i in range(count)])


RING = 4
TILE_ROWS = 16


def ring_gather(rows, stride, count, split):
    def step(cells, delta):
        pairs = []
        for i in range(count):
            coord = (i // stride) % RING
            pairs.append((i, i + (((coord + delta) % RING) - coord) * stride))
        return lax.ppermute(cells, "band", pairs)

    left = step(rows, 1)
    right = step(rows, -1)
    if split:
        half = rows.shape[0] // 2
        return jnp.concatenate([rows, left, right, step(left[:half], 1), step(right[half:], -1)])
    return jnp.concatenate([rows, left, right, step(left, 1)])


def _scatter_body(blk_ref, spread_ref, out_ref, acc_ref):
    bands = out_ref.shape[0]
    blocks = out_ref.shape[1]
    group = spread_ref.shape[0]
    g = pl.program_id(0)

    @pl.when(g == 0)
    def _():
        acc_ref[...] = jnp.zeros(acc_ref.shape, jnp.float32)

    def step(p, carry):
        row = pl.multiple_of(blk_ref[g * group + p] * bands, bands)
        acc_ref[pl.ds(row, bands), :] += spread_ref[p]
        return carry

    lax.fori_loop(0, group, step, 0, unroll=2)

    @pl.when(g == pl.num_programs(0) - 1)
    def _():
        def emit(n, carry):
            out_ref[n] = acc_ref[pl.ds(n, blocks, stride=bands), :].astype(out_ref.dtype)
            return carry

        lax.fori_loop(0, bands, emit, 0)


GROUP = 64


def scatter_blocks(index_block, spread, block_count):
    pieces, bands, width = spread.shape
    return pl.pallas_call(
        _scatter_body,
        out_shape=jax.ShapeDtypeStruct((bands, block_count, width), jnp.bfloat16),
        grid_spec=pltpu.PrefetchScalarGridSpec(
            num_scalar_prefetch=1,
            grid=(pieces // GROUP,),
            in_specs=[pl.BlockSpec((GROUP, bands, width), lambda g, blk: (g, 0, 0))],
            out_specs=pl.BlockSpec((bands, block_count, width), lambda g, blk: (0, 0, 0)),
            scratch_shapes=[pltpu.VMEM((block_count * bands, width), jnp.float32)],
        ),
        compiler_params=pltpu.CompilerParams(vmem_limit_bytes=48 * 1024 * 1024),
    )(index_block, spread)


def body(orbitals, projectors, piece_block, piece_atom, coupling):
    slab_waves = lax.all_to_all(orbitals, "band", split_axis=1, concat_axis=0, tiled=True)
    band_count = slab_waves.shape[0]
    blocks = slab_waves.reshape(band_count, -1, BLOCK)
    block_count = blocks.shape[1]
    proj_local = projectors[0, 0]
    index_block = piece_block[0, 0]
    index_atom = piece_atom[0, 0]
    pieces = index_block.shape[0]
    slot_count = coupling.shape[0]
    is_live = index_atom >= 0
    picked = jnp.take(blocks, index_block, axis=1)
    projected = jnp.einsum("pjk,npk->pjn", proj_local, picked, preferred_element_type=jnp.float32)
    target = jnp.where(is_live, index_atom, 3 * slot_count)
    partial_value = jax.ops.segment_sum(
        projected.reshape(pieces, -1), target, num_segments=3 * slot_count + 1
    )
    partial_value = partial_value[: 3 * slot_count].reshape(3, slot_count, -1)
    own_total = (
        partial_value[1]
        + shift(partial_value[0], "slab", -1)
        + shift(partial_value[2], "slab", 1)
    )
    band_size = lax.axis_size("band")
    share = slot_count // band_size
    arrived = lax.all_to_all(
        own_total.reshape(band_size, share, -1), "band", split_axis=0, concat_axis=0, tiled=True
    )
    mine = arrived.sum(axis=0)
    first = lax.axis_index("band") * share
    matrices = lax.dynamic_slice_in_dim(coupling, first, share, axis=0).reshape(share, PROJ, PROJ)
    dressed = jnp.einsum(
        "aij,ajn->ain",
        matrices,
        mine.reshape(share, PROJ, band_count),
        precision=lax.Precision.HIGHEST,
    ).astype(jnp.bfloat16).reshape(share, PROJ * band_count)
    every = jnp.concatenate([shift(dressed, "slab", 1), dressed, shift(dressed, "slab", -1)])
    block_rows = -(-every.shape[0] // TILE_ROWS) * TILE_ROWS
    every = jnp.pad(every, ((0, block_rows - every.shape[0]), (0, 0)))
    every = ring_gather(every, 1, band_size, False)
    every = ring_gather(every, RING, band_size, True)
    side_of = index_atom // slot_count
    slot_of = index_atom % slot_count
    source = slot_of // share
    me = lax.axis_index("band")
    order = jnp.array([0, 2, 3, 1], jnp.int32)
    place_x = order[(source % RING - me % RING) % RING]
    place_y = order[(source // RING - me // RING) % RING]
    place = place_y * RING + place_x
    row_of = place * block_rows + side_of * share + slot_of % share
    chosen = jnp.take(every, jnp.where(is_live, row_of, 0), axis=0)
    chosen = jnp.where(is_live[:, None], chosen, jnp.zeros((), jnp.bfloat16))
    chosen = chosen.reshape(pieces, PROJ, band_count)
    spread = jnp.einsum("pjk,pjn->pnk", proj_local, chosen, preferred_element_type=jnp.float32)
    result = scatter_blocks(index_block, spread, block_count)
    result = result.reshape(band_count, -1)
    return lax.all_to_all(result, "band", split_axis=0, concat_axis=1, tiled=True)


def solution(mesh):
    placed = (
        P("band", "slab"),
        P("slab", "band", None, None, None),
        P("slab", "band", None),
        P("slab", "band", None),
        P("slab", None),
    )
    return jax.shard_map(
        body, mesh=mesh, in_specs=placed, out_specs=P("band", "slab"), check_vma=False
    )
```

```python
import jax
import jax.numpy as jnp
from jax import lax
from jax.experimental import pallas as pl
from jax.experimental.pallas import tpu as pltpu
from jax.sharding import PartitionSpec as P

PROJ = 18
BLOCK = 128


def shift(cells, axis, step):
    count = lax.axis_size(axis)
    return lax.ppermute(cells, axis, [(i, (i + step) % count) for i in range(count)])


RING = 4
TILE_ROWS = 16


def ring_gather(rows, stride, count, split):
    def step(cells, delta):
        pairs = []
        for i in range(count):
            coord = (i // stride) % RING
            pairs.append((i, i + (((coord + delta) % RING) - coord) * stride))
        return lax.ppermute(cells, "band", pairs)

    left = step(rows, 1)
    right = step(rows, -1)
    if split:
        half = rows.shape[0] // 2
        return jnp.concatenate([rows, left, right, step(left[:half], 1), step(right[half:], -1)])
    return jnp.concatenate([rows, left, right, step(left, 1)])


def _scatter_body(blk_ref, spread_ref, out_ref, acc_ref):
    bands = out_ref.shape[0]
    blocks = out_ref.shape[1]
    acc_ref[...] = jnp.zeros(acc_ref.shape, jnp.float32)

    def step(p, carry):
        row = pl.multiple_of(blk_ref[p] * bands, bands)
        acc_ref[pl.ds(row, bands), :] += spread_ref[p]
        return carry

    lax.fori_loop(0, spread_ref.shape[0], step, 0, unroll=8)
    def emit(n, carry):
        out_ref[n] = acc_ref[pl.ds(n, blocks, stride=bands), :].astype(out_ref.dtype)
        return carry

    lax.fori_loop(0, bands, emit, 0)


def scatter_blocks(index_block, spread, block_count):
    pieces, bands, width = spread.shape
    return pl.pallas_call(
        _scatter_body,
        out_shape=jax.ShapeDtypeStruct((bands, block_count, width), jnp.bfloat16),
        in_specs=[
            pl.BlockSpec(memory_space=pltpu.SMEM),
            pl.BlockSpec(memory_space=pltpu.VMEM),
        ],
        out_specs=pl.BlockSpec(memory_space=pltpu.VMEM),
        scratch_shapes=[pltpu.VMEM((block_count * bands, width), jnp.float32)],
        compiler_params=pltpu.CompilerParams(vmem_limit_bytes=48 * 1024 * 1024),
    )(index_block, spread)


def body(orbitals, projectors, piece_block, piece_atom, coupling):
    slab_waves = lax.all_to_all(orbitals, "band", split_axis=1, concat_axis=0, tiled=True)
    band_count = slab_waves.shape[0]
    blocks = slab_waves.reshape(band_count, -1, BLOCK)
    block_count = blocks.shape[1]
    proj_local = projectors[0, 0]
    index_block = piece_block[0, 0]
    index_atom = piece_atom[0, 0]
    pieces = index_block.shape[0]
    slot_count = coupling.shape[0]
    is_live = index_atom >= 0
    picked = jnp.take(blocks, index_block, axis=1)
    projected = jnp.einsum("pjk,npk->pjn", proj_local, picked, preferred_element_type=jnp.float32)
    target = jnp.where(is_live, index_atom, 3 * slot_count)
    partial_value = jax.ops.segment_sum(
        projected.reshape(pieces, -1), target, num_segments=3 * slot_count + 1
    )
    partial_value = partial_value[: 3 * slot_count].reshape(3, slot_count, -1)
    own_total = (
        partial_value[1]
        + shift(partial_value[0], "slab", -1)
        + shift(partial_value[2], "slab", 1)
    )
    band_size = lax.axis_size("band")
    share = slot_count // band_size
    arrived = lax.all_to_all(
        own_total.reshape(band_size, share, -1), "band", split_axis=0, concat_axis=0, tiled=True
    )
    mine = arrived.sum(axis=0)
    first = lax.axis_index("band") * share
    matrices = lax.dynamic_slice_in_dim(coupling, first, share, axis=0).reshape(share, PROJ, PROJ)
    dressed = jnp.einsum(
        "aij,ajn->ain",
        matrices,
        mine.reshape(share, PROJ, band_count),
        precision=lax.Precision.HIGHEST,
    ).astype(jnp.bfloat16).reshape(share, PROJ * band_count)
    every = jnp.concatenate([shift(dressed, "slab", 1), dressed, shift(dressed, "slab", -1)])
    block_rows = -(-every.shape[0] // TILE_ROWS) * TILE_ROWS
    every = jnp.pad(every, ((0, block_rows - every.shape[0]), (0, 0)))
    every = ring_gather(every, 1, band_size, False)
    every = ring_gather(every, RING, band_size, True)
    side_of = index_atom // slot_count
    slot_of = index_atom % slot_count
    source = slot_of // share
    me = lax.axis_index("band")
    order = jnp.array([0, 2, 3, 1], jnp.int32)
    place_x = order[(source % RING - me % RING) % RING]
    place_y = order[(source // RING - me // RING) % RING]
    place = place_y * RING + place_x
    row_of = place * block_rows + side_of * share + slot_of % share
    chosen = jnp.take(every, jnp.where(is_live, row_of, 0), axis=0)
    chosen = jnp.where(is_live[:, None], chosen, jnp.zeros((), jnp.bfloat16))
    chosen = chosen.reshape(pieces, PROJ, band_count)
    spread = jnp.einsum("pjk,pjn->pnk", proj_local, chosen, preferred_element_type=jnp.float32)
    result = scatter_blocks(index_block, spread, block_count)
    result = result.reshape(band_count, -1)
    return lax.all_to_all(result, "band", split_axis=0, concat_axis=1, tiled=True)


def solution(mesh):
    placed = (
        P("band", "slab"),
        P("slab", "band", None, None, None),
        P("slab", "band", None),
        P("slab", "band", None),
        P("slab", None),
    )
    return jax.shard_map(
        body, mesh=mesh, in_specs=placed, out_specs=P("band", "slab"), check_vma=False
    )
```

```python
import jax
import jax.numpy as jnp
from jax import lax
from jax.experimental import pallas as pl
from jax.experimental.pallas import tpu as pltpu
from jax.sharding import PartitionSpec as P

PROJ = 18
BLOCK = 128


def shift(cells, axis, step):
    count = lax.axis_size(axis)
    return lax.ppermute(cells, axis, [(i, (i + step) % count) for i in range(count)])


RING = 4
TILE_ROWS = 16


def ring_gather(rows, stride, count, split):
    def step(cells, delta):
        pairs = []
        for i in range(count):
            coord = (i // stride) % RING
            pairs.append((i, i + (((coord + delta) % RING) - coord) * stride))
        return lax.ppermute(cells, "band", pairs)

    left = step(rows, 1)
    right = step(rows, -1)
    if split:
        half = rows.shape[0] // 2
        return jnp.concatenate([rows, left, right, step(left[:half], 1), step(right[half:], -1)])
    return jnp.concatenate([rows, left, right, step(left, 1)])


def _scatter_body(blk_ref, spread_ref, out_ref, acc_ref):
    bands = out_ref.shape[0]
    blocks = out_ref.shape[1]
    acc_ref[...] = jnp.zeros(acc_ref.shape, jnp.float32)

    def step(p, carry):
        row = pl.multiple_of(blk_ref[p] * bands, bands)
        acc_ref[pl.ds(row, bands), :] += spread_ref[p]
        return carry

    lax.fori_loop(0, spread_ref.shape[0], step, 0, unroll=8)
    def emit(n, carry):
        out_ref[n] = acc_ref[pl.ds(n, blocks, stride=bands), :].astype(out_ref.dtype)
        return carry

    lax.fori_loop(0, bands, emit, 0)


def scatter_blocks(index_block, spread, block_count):
    pieces, bands, width = spread.shape
    return pl.pallas_call(
        _scatter_body,
        out_shape=jax.ShapeDtypeStruct((bands, block_count, width), jnp.bfloat16),
        in_specs=[
            pl.BlockSpec(memory_space=pltpu.SMEM),
            pl.BlockSpec(memory_space=pltpu.VMEM),
        ],
        out_specs=pl.BlockSpec(memory_space=pltpu.VMEM),
        scratch_shapes=[pltpu.VMEM((block_count * bands, width), jnp.float32)],
        compiler_params=pltpu.CompilerParams(vmem_limit_bytes=48 * 1024 * 1024),
    )(index_block, spread)


def body(orbitals, projectors, piece_block, piece_atom, coupling):
    slab_waves = lax.all_to_all(orbitals, "band", split_axis=1, concat_axis=0, tiled=True)
    band_count = slab_waves.shape[0]
    blocks = slab_waves.reshape(band_count, -1, BLOCK)
    block_count = blocks.shape[1]
    proj_local = projectors[0, 0]
    index_block = piece_block[0, 0]
    index_atom = piece_atom[0, 0]
    pieces = index_block.shape[0]
    slot_count = coupling.shape[0]
    is_live = index_atom >= 0
    onehot = (index_block[:, None] == jnp.arange(block_count)[None, :]).astype(jnp.bfloat16)
    picked = jnp.einsum(
        "pb,nbk->npk", onehot, blocks, preferred_element_type=jnp.float32
    ).astype(jnp.bfloat16)
    projected = jnp.einsum("pjk,npk->pjn", proj_local, picked, preferred_element_type=jnp.float32)
    target = jnp.where(is_live, index_atom, 3 * slot_count)
    partial_value = jax.ops.segment_sum(
        projected.reshape(pieces, -1), target, num_segments=3 * slot_count + 1
    )
    partial_value = partial_value[: 3 * slot_count].reshape(3, slot_count, -1)
    own_total = (
        partial_value[1]
        + shift(partial_value[0], "slab", -1)
        + shift(partial_value[2], "slab", 1)
    )
    band_size = lax.axis_size("band")
    share = slot_count // band_size
    arrived = lax.all_to_all(
        own_total.reshape(band_size, share, -1), "band", split_axis=0, concat_axis=0, tiled=True
    )
    mine = arrived.sum(axis=0)
    first = lax.axis_index("band") * share
    matrices = lax.dynamic_slice_in_dim(coupling, first, share, axis=0).reshape(share, PROJ, PROJ)
    dressed = jnp.einsum(
        "aij,ajn->ain",
        matrices,
        mine.reshape(share, PROJ, band_count),
        precision=lax.Precision.HIGHEST,
    ).astype(jnp.bfloat16).reshape(share, PROJ * band_count)
    every = jnp.concatenate([shift(dressed, "slab", 1), dressed, shift(dressed, "slab", -1)])
    block_rows = -(-every.shape[0] // TILE_ROWS) * TILE_ROWS
    every = jnp.pad(every, ((0, block_rows - every.shape[0]), (0, 0)))
    every = ring_gather(every, 1, band_size, False)
    every = ring_gather(every, RING, band_size, True)
    side_of = index_atom // slot_count
    slot_of = index_atom % slot_count
    source = slot_of // share
    me = lax.axis_index("band")
    order = jnp.array([0, 2, 3, 1], jnp.int32)
    place_x = order[(source % RING - me % RING) % RING]
    place_y = order[(source // RING - me // RING) % RING]
    place = place_y * RING + place_x
    row_of = place * block_rows + side_of * share + slot_of % share
    chosen = jnp.take(every, jnp.where(is_live, row_of, 0), axis=0)
    chosen = jnp.where(is_live[:, None], chosen, jnp.zeros((), jnp.bfloat16))
    chosen = chosen.reshape(pieces, PROJ, band_count)
    spread = jnp.einsum("pjk,pjn->pnk", proj_local, chosen, preferred_element_type=jnp.float32)
    result = scatter_blocks(index_block, spread, block_count)
    result = result.reshape(band_count, -1)
    return lax.all_to_all(result, "band", split_axis=0, concat_axis=1, tiled=True)


def solution(mesh):
    placed = (
        P("band", "slab"),
        P("slab", "band", None, None, None),
        P("slab", "band", None),
        P("slab", "band", None),
        P("slab", None),
    )
    return jax.shard_map(
        body, mesh=mesh, in_specs=placed, out_specs=P("band", "slab"), check_vma=False
    )
```

```python
import jax
import jax.numpy as jnp
from jax import lax
from jax.experimental import pallas as pl
from jax.experimental.pallas import tpu as pltpu
from jax.sharding import PartitionSpec as P

PROJ = 18
BLOCK = 128


def shift(cells, axis, step):
    count = lax.axis_size(axis)
    return lax.ppermute(cells, axis, [(i, (i + step) % count) for i in range(count)])


RING = 4
TILE_ROWS = 16


def ring_gather(rows, stride, count, split):
    def step(cells, delta):
        pairs = []
        for i in range(count):
            coord = (i // stride) % RING
            pairs.append((i, i + (((coord + delta) % RING) - coord) * stride))
        return lax.ppermute(cells, "band", pairs)

    left = step(rows, 1)
    right = step(rows, -1)
    if split:
        half = rows.shape[0] // 2
        return jnp.concatenate([rows, left, right, step(left[:half], 1), step(right[half:], -1)])
    return jnp.concatenate([rows, left, right, step(left, 1)])


def _scatter_body(blk_ref, spread_ref, out_ref, acc_ref):
    bands = out_ref.shape[0]
    blocks = out_ref.shape[1]
    acc_ref[...] = jnp.zeros(acc_ref.shape, jnp.float32)

    def step(p, carry):
        row = pl.multiple_of(blk_ref[p] * bands, bands)
        acc_ref[pl.ds(row, bands), :] += spread_ref[p]
        return carry

    lax.fori_loop(0, spread_ref.shape[0], step, 0, unroll=8)
    def emit(n, carry):
        out_ref[n] = acc_ref[pl.ds(n, blocks, stride=bands), :].astype(out_ref.dtype)
        return carry

    lax.fori_loop(0, bands, emit, 0)


def scatter_blocks(index_block, spread, block_count):
    pieces, bands, width = spread.shape
    return pl.pallas_call(
        _scatter_body,
        out_shape=jax.ShapeDtypeStruct((bands, block_count, width), jnp.bfloat16),
        in_specs=[
            pl.BlockSpec(memory_space=pltpu.SMEM),
            pl.BlockSpec(memory_space=pltpu.VMEM),
        ],
        out_specs=pl.BlockSpec(memory_space=pltpu.VMEM),
        scratch_shapes=[pltpu.VMEM((block_count * bands, width), jnp.float32)],
        compiler_params=pltpu.CompilerParams(vmem_limit_bytes=48 * 1024 * 1024),
    )(index_block, spread)


def body(orbitals, projectors, piece_block, piece_atom, coupling):
    slab_waves = lax.all_to_all(orbitals, "band", split_axis=1, concat_axis=0, tiled=True)
    band_count = slab_waves.shape[0]
    blocks = slab_waves.reshape(band_count, -1, BLOCK)
    block_count = blocks.shape[1]
    proj_local = projectors[0, 0]
    index_block = piece_block[0, 0]
    index_atom = piece_atom[0, 0]
    pieces = index_block.shape[0]
    slot_count = coupling.shape[0]
    is_live = index_atom >= 0
    onehot = (index_block[:, None] == jnp.arange(block_count)[None, :]).astype(jnp.bfloat16)
    picked = jnp.einsum(
        "pb,nbk->npk", onehot, blocks, preferred_element_type=jnp.float32
    ).astype(jnp.bfloat16)
    projected = jnp.einsum("pjk,npk->pjn", proj_local, picked, preferred_element_type=jnp.float32)
    target = jnp.where(is_live, index_atom, 3 * slot_count)
    partial_value = jax.ops.segment_sum(
        projected.reshape(pieces, -1), target, num_segments=3 * slot_count + 1
    )
    partial_value = partial_value[: 3 * slot_count].reshape(3, slot_count, -1)
    own_total = (
        partial_value[1]
        + shift(partial_value[0], "slab", -1)
        + shift(partial_value[2], "slab", 1)
    )
    band_size = lax.axis_size("band")
    share = slot_count // band_size
    arrived = lax.all_to_all(
        own_total.reshape(band_size, share, -1), "band", split_axis=0, concat_axis=0, tiled=True
    )
    mine = arrived.sum(axis=0)
    first = lax.axis_index("band") * share
    matrices = lax.dynamic_slice_in_dim(coupling, first, share, axis=0).reshape(share, PROJ, PROJ)
    dressed = jnp.einsum(
        "aij,ajn->ain",
        matrices,
        mine.reshape(share, PROJ, band_count),
        precision=lax.Precision.HIGHEST,
    ).astype(jnp.bfloat16).reshape(share, PROJ * band_count)
    every = jnp.concatenate([shift(dressed, "slab", 1), dressed, shift(dressed, "slab", -1)])
    block_rows = -(-every.shape[0] // TILE_ROWS) * TILE_ROWS
    every = jnp.pad(every, ((0, block_rows - every.shape[0]), (0, 0)))
    every = ring_gather(every, 1, band_size, False)
    every = ring_gather(every, RING, band_size, True)
    side_of = index_atom // slot_count
    slot_of = index_atom % slot_count
    source = slot_of // share
    me = lax.axis_index("band")
    order = jnp.array([0, 2, 3, 1], jnp.int32)
    place_x = order[(source % RING - me % RING) % RING]
    place_y = order[(source // RING - me // RING) % RING]
    place = place_y * RING + place_x
    row_of = place * block_rows + side_of * share + slot_of % share
    pick = (row_of[:, None] == jnp.arange(every.shape[0])[None, :]) & is_live[:, None]
    chosen = jnp.einsum(
        "pr,rc->pc", pick.astype(jnp.bfloat16), every, preferred_element_type=jnp.float32
    ).astype(jnp.bfloat16)
    chosen = chosen.reshape(pieces, PROJ, band_count)
    spread = jnp.einsum("pjk,pjn->pnk", proj_local, chosen, preferred_element_type=jnp.float32)
    result = scatter_blocks(index_block, spread, block_count)
    result = result.reshape(band_count, -1)
    return lax.all_to_all(result, "band", split_axis=0, concat_axis=1, tiled=True)


def solution(mesh):
    placed = (
        P("band", "slab"),
        P("slab", "band", None, None, None),
        P("slab", "band", None),
        P("slab", "band", None),
        P("slab", None),
    )
    return jax.shard_map(
        body, mesh=mesh, in_specs=placed, out_specs=P("band", "slab"), check_vma=False
    )
```

```python
import jax
import jax.numpy as jnp
from jax import lax
from jax.experimental import pallas as pl
from jax.experimental.pallas import tpu as pltpu
from jax.sharding import PartitionSpec as P

PROJ = 18
BLOCK = 128


def shift(cells, axis, step):
    count = lax.axis_size(axis)
    return lax.ppermute(cells, axis, [(i, (i + step) % count) for i in range(count)])


RING = 4
TILE_ROWS = 16


def ring_gather(rows, stride, count, split):
    def step(cells, delta):
        pairs = []
        for i in range(count):
            coord = (i // stride) % RING
            pairs.append((i, i + (((coord + delta) % RING) - coord) * stride))
        return lax.ppermute(cells, "band", pairs)

    left = step(rows, 1)
    right = step(rows, -1)
    if split:
        half = rows.shape[0] // 2
        return jnp.concatenate([rows, left, right, step(left[:half], 1), step(right[half:], -1)])
    return jnp.concatenate([rows, left, right, step(left, 1)])


def _scatter_body(blk_ref, spread_ref, out_ref, acc_ref):
    bands = out_ref.shape[0]
    blocks = out_ref.shape[1]
    acc_ref[...] = jnp.zeros(acc_ref.shape, jnp.float32)

    def step(p, carry):
        row = pl.multiple_of(blk_ref[p] * bands, bands)
        acc_ref[pl.ds(row, bands), :] += spread_ref[p]
        return carry

    lax.fori_loop(0, spread_ref.shape[0], step, 0, unroll=8)
    def emit(n, carry):
        out_ref[n] = acc_ref[pl.ds(n, blocks, stride=bands), :].astype(out_ref.dtype)
        return carry

    lax.fori_loop(0, bands, emit, 0)


def scatter_blocks(index_block, spread, block_count):
    pieces, bands, width = spread.shape
    return pl.pallas_call(
        _scatter_body,
        out_shape=jax.ShapeDtypeStruct((bands, block_count, width), jnp.bfloat16),
        in_specs=[
            pl.BlockSpec(memory_space=pltpu.SMEM),
            pl.BlockSpec(memory_space=pltpu.VMEM),
        ],
        out_specs=pl.BlockSpec(memory_space=pltpu.VMEM),
        scratch_shapes=[pltpu.VMEM((block_count * bands, width), jnp.float32)],
        compiler_params=pltpu.CompilerParams(vmem_limit_bytes=48 * 1024 * 1024),
    )(index_block, spread)


def body(orbitals, projectors, piece_block, piece_atom, coupling):
    slab_waves = lax.all_to_all(orbitals, "band", split_axis=1, concat_axis=0, tiled=True)
    band_count = slab_waves.shape[0]
    blocks = slab_waves.reshape(band_count, -1, BLOCK)
    block_count = blocks.shape[1]
    proj_local = projectors[0, 0]
    index_block = piece_block[0, 0]
    index_atom = piece_atom[0, 0]
    pieces = index_block.shape[0]
    slot_count = coupling.shape[0]
    is_live = index_atom >= 0
    onehot = (index_block[:, None] == jnp.arange(block_count)[None, :]).astype(jnp.bfloat16)
    picked = jnp.einsum(
        "pb,nbk->npk", onehot, blocks, preferred_element_type=jnp.float32
    ).astype(jnp.bfloat16)
    projected = jnp.einsum("pjk,npk->pjn", proj_local, picked, preferred_element_type=jnp.float32)
    target = jnp.where(is_live, index_atom, 3 * slot_count)
    gather_atom = (jnp.arange(3 * slot_count)[:, None] == target[None, :]).astype(jnp.float32)
    partial_value = jnp.einsum(
        "ap,pc->ac", gather_atom, projected.reshape(pieces, -1), precision=lax.Precision.HIGHEST
    )
    partial_value = partial_value[: 3 * slot_count].reshape(3, slot_count, -1)
    own_total = (
        partial_value[1]
        + shift(partial_value[0], "slab", -1)
        + shift(partial_value[2], "slab", 1)
    )
    band_size = lax.axis_size("band")
    share = slot_count // band_size
    arrived = lax.all_to_all(
        own_total.reshape(band_size, share, -1), "band", split_axis=0, concat_axis=0, tiled=True
    )
    mine = arrived.sum(axis=0)
    first = lax.axis_index("band") * share
    matrices = lax.dynamic_slice_in_dim(coupling, first, share, axis=0).reshape(share, PROJ, PROJ)
    dressed = jnp.einsum(
        "aij,ajn->ain",
        matrices,
        mine.reshape(share, PROJ, band_count),
        precision=lax.Precision.HIGHEST,
    ).astype(jnp.bfloat16).reshape(share, PROJ * band_count)
    every = jnp.concatenate([shift(dressed, "slab", 1), dressed, shift(dressed, "slab", -1)])
    block_rows = -(-every.shape[0] // TILE_ROWS) * TILE_ROWS
    every = jnp.pad(every, ((0, block_rows - every.shape[0]), (0, 0)))
    every = ring_gather(every, 1, band_size, False)
    every = ring_gather(every, RING, band_size, True)
    side_of = index_atom // slot_count
    slot_of = index_atom % slot_count
    source = slot_of // share
    me = lax.axis_index("band")
    order = jnp.array([0, 2, 3, 1], jnp.int32)
    place_x = order[(source % RING - me % RING) % RING]
    place_y = order[(source // RING - me // RING) % RING]
    place = place_y * RING + place_x
    row_of = place * block_rows + side_of * share + slot_of % share
    pick = (row_of[:, None] == jnp.arange(every.shape[0])[None, :]) & is_live[:, None]
    chosen = jnp.einsum(
        "pr,rc->pc", pick.astype(jnp.bfloat16), every, preferred_element_type=jnp.float32
    ).astype(jnp.bfloat16)
    chosen = chosen.reshape(pieces, PROJ, band_count)
    spread = jnp.einsum("pjk,pjn->pnk", proj_local, chosen, preferred_element_type=jnp.float32)
    result = scatter_blocks(index_block, spread, block_count)
    result = result.reshape(band_count, -1)
    return lax.all_to_all(result, "band", split_axis=0, concat_axis=1, tiled=True)


def solution(mesh):
    placed = (
        P("band", "slab"),
        P("slab", "band", None, None, None),
        P("slab", "band", None),
        P("slab", "band", None),
        P("slab", None),
    )
    return jax.shard_map(
        body, mesh=mesh, in_specs=placed, out_specs=P("band", "slab"), check_vma=False
    )
```
